32 devices in a mesh: groups: 2 (over x), slab: 16 (over z, y, core).
Axes of the slice: x: 2, y: 2, z: 4, core: 2. Of those that a mesh axis runs over, the one named last changes fastest.
Arguments:
- volume: bfloat16 [64, 48, 48, 128], P(('groups', 'slab')), parts along dimension 0, may hold values from -6 to 6
- kernel: bfloat16 [3, 3, 3, 128, 128], replicated, may hold values from -0.109375 to 0.109375
- grad_out: bfloat16 [64, 48, 48, 128], P(('groups', 'slab')), parts along dimension 0, may hold values from -6 to 6
Outputs:
- activation: bfloat16 [64, 48, 48, 128], P(('groups', 'slab')), parts along dimension 0
- input_grad: bfloat16 [64, 48, 48, 128], P(('groups', 'slab')), parts along dimension 0
- weight_grad: float32 [6, 3, 3, 128, 128], P('groups'), parts along dimension 0
The draws below stay inside these ranges and needn't reach their ends.
There are 2 independent parts, one for each index of `groups`. The reference program is written for one: setup_inputs(seed, part) draws one part's arguments, and reference() takes and returns one part's arrays. A program takes and returns all parts, laid end to end along the dimension named above; an argument that names none is the same for every part. Nothing has to cross between parts.
All inputs are finite; a program needn't handle non-finite values.
Results may differ from the reference program's by a relative error of at most 0.001.
Values may be sent and summed in bfloat16 or wider, within the bound.
No kernel may reach another device: no remote copies, remote signals or barrier semaphores. Data moves between devices by JAX's collectives and lax.ppermute only.
A program may use at most 64 MiB of HBM per device.

```python
import jax
import jax.numpy as jnp
from jax import lax

C = 128
HEIGHT = 48
BREADTH = 48
DEPTH = 32


def shard_levels(rng, dims, cuts, smallest, top_value):
    def one(dim, shards_of):
        steps = jax.random.uniform(jax.random.fold_in(jax.random.fold_in(rng, 6), dim), (shards_of,), jnp.float32, smallest / len(cuts), top_value / len(cuts))
        return jnp.repeat(jnp.exp(steps), dims[dim] // shards_of).reshape((-1,) + (1,) * (len(dims) - dim - 1))

    level = one(*cuts[0])
    for cut in cuts[1:]:
        level = level * one(*cut)
    return level


def bell_draw(key, shape, width, reach, pieces=(), kind=jnp.bfloat16):
    result = jax.random.normal(key, shape, jnp.float32) * width
    if len(pieces) > 0:
        result = shard_levels(key, shape, pieces, -0.22, 0.18) * result
    return jnp.clip(result, min=-reach, max=reach).astype(kind)


def setup_inputs(seed: int = 0, part: int = 0) -> dict:
    arg_keys = jax.random.split(jax.random.key(seed), 4)
    part_splits = jax.random.split(jax.random.fold_in(arg_keys[3], part), 4)
    volume = bell_draw(part_splits[0], (DEPTH, HEIGHT, BREADTH, C), 1.0, 6.0, ((0, 16),))
    kernel = bell_draw(arg_keys[1], (3, 3, 3, C, C), (27 * C) ** -0.5, 0.109375)
    grad_out = bell_draw(part_splits[2], (DEPTH, HEIGHT, BREADTH, C), 1.0, 6.0, ((0, 16),))
    return {"volume": volume, "kernel": kernel, "grad_out": grad_out}


def plane_conv(padded, kernel, plane):
    height = padded.shape[1] - 2
    breadth = padded.shape[2] - 2
    channels = padded.shape[3]
    window = lax.dynamic_slice_in_dim(padded, plane, 3, 0)
    total = jnp.zeros((height * breadth, kernel.shape[4]), jnp.float32)
    for depth_off in range(3):
        for row_off in range(3):
            for col_off in range(3):
                cells = window[depth_off, row_off:row_off + height, col_off:col_off + breadth, :]
                total = total + jnp.dot(cells.reshape(height * breadth, channels), kernel[depth_off, row_off, col_off], preferred_element_type=jnp.float32)
    return total.reshape(height, breadth, kernel.shape[4]).astype(jnp.bfloat16)

def full_conv(padded, kernel, depth):
    planes = jnp.arange(depth, dtype=jnp.int32)
    return lax.map(lambda plane: plane_conv(padded, kernel, plane), planes)

def reference(volume, kernel, grad_out):
    depth, height, breadth, channels = volume.shape
    padded = jnp.pad(volume, ((1, 1), (1, 1), (1, 1), (0, 0)))
    activation = full_conv(padded, kernel, depth)
    grad_padded = jnp.pad(grad_out, ((1, 1), (1, 1), (1, 1), (0, 0)))
    flipped = jnp.swapaxes(kernel[::-1, ::-1, ::-1], 3, 4)
    input_grad = full_conv(grad_padded, flipped, depth)

    def accumulate(carry, plane):
        window = lax.dynamic_slice_in_dim(padded, plane, 3, 0)
        grads = lax.dynamic_slice_in_dim(grad_out, plane, 1, 0)[0].reshape(height * breadth, channels)
        rows = []
        for depth_off in range(3):
            for row_off in range(3):
                for col_off in range(3):
                    cells = window[depth_off, row_off:row_off + height, col_off:col_off + breadth, :]
                    cells = cells.reshape(height * breadth, channels)
                    rows.append(jnp.dot(cells.T, grads, preferred_element_type=jnp.float32))
        update = jnp.stack(rows).reshape(3, 3, 3, channels, channels)
        return (carry + update, None)
    start = jnp.zeros((3, 3, 3, channels, channels), jnp.float32)
    summed, _ = lax.scan(accumulate, start, jnp.arange(depth, dtype=jnp.int32))
    cells_all = depth * height * breadth
    weight_grad = summed / jnp.sqrt(jnp.float32(cells_all))
    return (activation, input_grad, weight_grad)
```

```python
import jax
import jax.numpy as jnp
from jax import lax
from jax.sharding import PartitionSpec as P


def extended_2(shard, sides, width):
    for axis, dim in sides:
        count, length = (lax.axis_size(axis), shard.shape[dim])
        up = [(i, (i + 1) % count) for i in range(count - 1)]
        down = [(j, i) for i, j in up]
        last = lax.slice_in_dim(shard, length - width, length, axis=dim)
        leading = lax.slice_in_dim(shard, 0, width, axis=dim)
        before = lax.ppermute(last, axis, up)
        after = lax.ppermute(leading, axis, down)
        shard = jnp.concatenate([before, shard, after], axis=dim)
    return shard


def conv_planes(padded, kernel):
    out = lax.conv_general_dilated(
        padded[None],
        kernel,
        (1, 1, 1),
        "VALID",
        dimension_numbers=("NDHWC", "DHWIO", "NDHWC"),
        preferred_element_type=jnp.float32,
    )
    return out[0]


def weight_terms(padded, grads):
    out = lax.conv_general_dilated(
        padded[None],
        grads[None],
        (1, 1, 1),
        "VALID",
        dimension_numbers=("CDHWN", "IDHWO", "NDHWC"),
        preferred_element_type=jnp.float32,
    )
    return jnp.transpose(out, (1, 2, 3, 0, 4))


def pad_sides(field):
    return jnp.pad(field, ((0, 0), (1, 1), (1, 1), (0, 0)))


def halving_sum(x, axis):
    count = lax.axis_size(axis)
    me = lax.axis_index(axis)
    bits = count.bit_length() - 1
    assert 1 << bits == count
    shape = x.shape
    flat = x.reshape(-1, shape[-1])
    rows = flat.shape[0]
    unit = count * 8
    padded_rows = -(-rows // unit) * unit
    flat = jnp.pad(flat, ((0, padded_rows - rows), (0, 0)))
    for k in range(bits):
        half = flat.shape[0] // 2
        bit = (me >> k) & 1
        keep = lax.dynamic_slice_in_dim(flat, bit * half, half, 0)
        send = lax.dynamic_slice_in_dim(flat, (1 - bit) * half, half, 0)
        pairs = [(i, i ^ (1 << k)) for i in range(count)]
        flat = keep + lax.ppermute(send, axis, pairs)
    for k in reversed(range(bits)):
        bit = (me >> k) & 1
        pairs = [(i, i ^ (1 << k)) for i in range(count)]
        other = lax.ppermute(flat, axis, pairs)
        low = jnp.where(bit == 0, flat, other)
        high = jnp.where(bit == 0, other, flat)
        flat = jnp.concatenate([low, high], 0)
    return flat[:rows].reshape(shape)


def body(volume, kernel, grad_out):
    stacked = jnp.stack((volume, grad_out))
    extended = extended_2(stacked, (("slab", 1),), 1)
    volume_ext = extended[0]
    grad_ext = extended[1]
    padded = pad_sides(volume_ext)
    grad_padded = pad_sides(grad_ext)
    activation = conv_planes(padded, kernel).astype(jnp.bfloat16)
    flipped = jnp.swapaxes(kernel[::-1, ::-1, ::-1], 3, 4)
    cells = lax.axis_size("slab") * grad_out.shape[0] * grad_out.shape[1] * grad_out.shape[2]
    factor = 1.0 / jnp.sqrt(jnp.float32(cells))
    terms = weight_terms(padded, grad_out)
    weight_grad = halving_sum(terms, "slab") * factor
    input_grad = conv_planes(grad_padded, flipped).astype(jnp.bfloat16)
    return (activation, input_grad, weight_grad)


def solution(mesh):
    return jax.shard_map(
        body,
        mesh=mesh,
        in_specs=(
            P(("groups", "slab"), None, None, None),
            P(),
            P(("groups", "slab"), None, None, None),
        ),
        out_specs=(
            P(("groups", "slab"), None, None, None),
            P(("groups", "slab"), None, None, None),
            P("groups", None, None, None, None),
        ),
        check_vma=False,
    )
```

```python
import jax
import jax.numpy as jnp
from jax import lax
from jax.sharding import PartitionSpec as P


def neighbour_planes(shard, axis):
    count = lax.axis_size(axis)
    up = [(i, i + 1) for i in range(count - 1)]
    down = [(j, i) for i, j in up]
    below = lax.ppermute(shard[:, -1:], axis, up)
    above = lax.ppermute(shard[:, :1], axis, down)
    return below, above


def conv_valid(planes, kernel):
    out = lax.conv_general_dilated(
        planes[None],
        kernel,
        (1, 1, 1),
        "VALID",
        dimension_numbers=("NDHWC", "DHWIO", "NDHWC"),
        preferred_element_type=jnp.float32,
    )
    return out[0]


def pad_sides(field):
    return jnp.pad(field, ((0, 0), (1, 1), (1, 1), (0, 0)))


def conv_split(local, below, above, kernel):
    lo = conv_valid(local, kernel[1:3])[0] + conv_valid(below, kernel[0:1])[0]
    hi = conv_valid(local, kernel[0:2])[0] + conv_valid(above, kernel[2:3])[0]
    return jnp.stack((lo, hi)).astype(jnp.bfloat16)


def column_stack(padded):
    width = padded.shape[2] - 2
    return jnp.concatenate([padded[:, :, c:c + width, :] for c in range(3)], -1)


def weight_rows(local, halos, grads):
    height = grads.shape[1]
    xl = column_stack(local)
    xh = column_stack(halos)
    out = []
    for b in range(3):
        m = jnp.einsum("phwk,qhwo->pqko", xl[:, b:b + height], grads,
                       preferred_element_type=jnp.float32)
        mh = jnp.einsum("phwk,phwo->pko", xh[:, b:b + height], grads,
                        preferred_element_type=jnp.float32)
        out.append(jnp.stack((m[0, 1] + mh[0], m[0, 0] + m[1, 1], m[1, 0] + mh[1])))
    return jnp.stack(out, 1)


def halving_sum(x, axis):
    count = lax.axis_size(axis)
    me = lax.axis_index(axis)
    bits = count.bit_length() - 1
    assert 1 << bits == count
    shape = x.shape
    flat = x.reshape(-1, shape[-1])
    rows = flat.shape[0]
    unit = count * 8
    padded_rows = -(-rows // unit) * unit
    flat = jnp.pad(flat, ((0, padded_rows - rows), (0, 0)))
    for k in range(bits):
        half = flat.shape[0] // 2
        bit = (me >> k) & 1
        keep = lax.dynamic_slice_in_dim(flat, bit * half, half, 0)
        send = lax.dynamic_slice_in_dim(flat, (1 - bit) * half, half, 0)
        pairs = [(i, i ^ (1 << k)) for i in range(count)]
        flat = keep + lax.ppermute(send, axis, pairs)
    for k in reversed(range(bits)):
        bit = (me >> k) & 1
        pairs = [(i, i ^ (1 << k)) for i in range(count)]
        other = lax.ppermute(flat, axis, pairs)
        low = jnp.where(bit == 0, flat, other)
        high = jnp.where(bit == 0, other, flat)
        flat = jnp.concatenate([low, high], 0)
    return flat[:rows].reshape(shape)


def body(volume, kernel, grad_out):
    assert volume.shape[0] == 2
    stacked = jnp.stack((volume, grad_out))
    below, above = neighbour_planes(stacked, "slab")
    vol_p = pad_sides(volume)
    grad_p = pad_sides(grad_out)
    vol_below, vol_above = pad_sides(below[0]), pad_sides(above[0])
    grad_below, grad_above = pad_sides(below[1]), pad_sides(above[1])
    cells = lax.axis_size("slab") * grad_out.shape[0] * grad_out.shape[1] * grad_out.shape[2]
    factor = 1.0 / jnp.sqrt(jnp.float32(cells))
    rows = weight_rows(vol_p, jnp.concatenate((vol_below, vol_above)), grad_out)
    terms = rows.reshape(3, 3, 3, kernel.shape[3], kernel.shape[4])
    weight_grad = halving_sum(terms, "slab") * factor
    activation = conv_split(vol_p, vol_below, vol_above, kernel)
    flipped = jnp.swapaxes(kernel[::-1, ::-1, ::-1], 3, 4)
    input_grad = conv_split(grad_p, grad_below, grad_above, flipped)
    return (activation, input_grad, weight_grad)


def solution(mesh):
    return jax.shard_map(
        body,
        mesh=mesh,
        in_specs=(
            P(("groups", "slab"), None, None, None),
            P(),
            P(("groups", "slab"), None, None, None),
        ),
        out_specs=(
            P(("groups", "slab"), None, None, None),
            P(("groups", "slab"), None, None, None),
            P("groups", None, None, None, None),
        ),
        check_vma=False,
    )
```

```python
import jax
import jax.numpy as jnp
from jax import lax
from jax.sharding import PartitionSpec as P


def neighbour_planes(fields, axis):
    count = lax.axis_size(axis)
    up = [(i, i + 1) for i in range(count - 1)]
    down = [(j, i) for i, j in up]
    below = lax.ppermute(jnp.concatenate([f[-1:] for f in fields]), axis, up)
    above = lax.ppermute(jnp.concatenate([f[:1] for f in fields]), axis, down)
    return below, above


def conv_valid(planes, kernel):
    out = lax.conv_general_dilated(
        planes[None],
        kernel,
        (1, 1, 1),
        "VALID",
        dimension_numbers=("NDHWC", "DHWIO", "NDHWC"),
        preferred_element_type=jnp.float32,
    )
    return out[0]


def pad_sides(field):
    return jnp.pad(field, ((0, 0), (1, 1), (1, 1), (0, 0)))


def conv_split(local, below, above, kernel):
    lo = conv_valid(local, kernel[1:3])[0] + conv_valid(below, kernel[0:1])[0]
    hi = conv_valid(local, kernel[0:2])[0] + conv_valid(above, kernel[2:3])[0]
    return jnp.stack((lo, hi)).astype(jnp.bfloat16)


def column_stack(padded):
    width = padded.shape[2] - 2
    return jnp.concatenate([padded[:, :, c:c + width, :] for c in range(3)], -1)


def weight_rows(local, halos, grads):
    height = grads.shape[1]
    xl = column_stack(local)
    xh = column_stack(halos)
    out = []
    for b in range(3):
        m = jnp.einsum("phwk,qhwo->pqko", xl[:, b:b + height], grads,
                       preferred_element_type=jnp.float32)
        mh = jnp.einsum("phwk,phwo->pko", xh[:, b:b + height], grads,
                        preferred_element_type=jnp.float32)
        out.append(jnp.stack((m[0, 1] + mh[0], m[0, 0] + m[1, 1], m[1, 0] + mh[1])))
    return jnp.stack(out, 1)


def stage_orders(bits):
    rest = list(range(1, bits))
    split = len(rest) // 2
    return [0] + rest, [0] + rest[split:] + rest[:split]


def halving_sum(x, axis, riders):
    count = lax.axis_size(axis)
    me = lax.axis_index(axis)
    bits = count.bit_length() - 1
    assert 1 << bits == count
    order_a, order_b = stage_orders(bits)
    odd = me & 1
    shape = x.shape
    flat = x.reshape(-1, shape[-1])
    rows = flat.shape[0]
    unit = count * 8
    padded_rows = -(-rows // unit) * unit
    flat = jnp.pad(flat, ((0, padded_rows - rows), (0, 0)))
    def partner(i, step):
        k = order_b[step] if i & 1 else order_a[step]
        return i ^ (1 << k)
    def my_bit(step):
        return jnp.where(odd == 1, (me >> order_b[step]) & 1, (me >> order_a[step]) & 1)
    for step in range(bits):
        half = flat.shape[0] // 2
        bit = my_bit(step)
        keep = lax.dynamic_slice_in_dim(flat, bit * half, half, 0)
        send = lax.dynamic_slice_in_dim(flat, (1 - bit) * half, half, 0)
        if step == 0:
            send, riders = lax.optimization_barrier((send, riders))
        pairs = [(i, partner(i, step)) for i in range(count)]
        flat = keep + lax.ppermute(send, axis, pairs)
    for step in reversed(range(bits)):
        bit = my_bit(step)
        pairs = [(i, partner(i, step)) for i in range(count)]
        other = lax.ppermute(flat, axis, pairs)
        low = jnp.where(bit == 0, flat, other)
        high = jnp.where(bit == 0, other, flat)
        flat = jnp.concatenate([low, high], 0)
    return flat[:rows].reshape(shape), riders


def body(volume, kernel, grad_out):
    assert volume.shape[0] == 2
    below, above = neighbour_planes((volume, grad_out), "slab")
    vol_p = pad_sides(volume)
    grad_p = pad_sides(grad_out)
    vol_below, vol_above = pad_sides(below[0:1]), pad_sides(above[0:1])
    cells = lax.axis_size("slab") * grad_out.shape[0] * grad_out.shape[1] * grad_out.shape[2]
    factor = 1.0 / jnp.sqrt(jnp.float32(cells))
    rows = weight_rows(vol_p, jnp.concatenate((vol_below, vol_above)), grad_out)
    terms = rows.reshape(3, 3, 3, kernel.shape[3], kernel.shape[4])
    riders = (vol_p, grad_p, vol_below, vol_above, below, above, kernel)
    summed, riders = halving_sum(terms, "slab", riders)
    vol_p, grad_p, vol_below, vol_above, below, above, kernel = riders
    weight_grad = summed * factor
    grad_below, grad_above = pad_sides(below[1:2]), pad_sides(above[1:2])
    activation = conv_split(vol_p, vol_below, vol_above, kernel)
    flipped = jnp.swapaxes(kernel[::-1, ::-1, ::-1], 3, 4)
    input_grad = conv_split(grad_p, grad_below, grad_above, flipped)
    return (activation, input_grad, weight_grad)


def solution(mesh):
    return jax.shard_map(
        body,
        mesh=mesh,
        in_specs=(
            P(("groups", "slab"), None, None, None),
            P(),
            P(("groups", "slab"), None, None, None),
        ),
        out_specs=(
            P(("groups", "slab"), None, None, None),
            P(("groups", "slab"), None, None, None),
            P("groups", None, None, None, None),
        ),
        check_vma=False,
    )
```

```python
import jax
import jax.numpy as jnp
from jax import lax
from jax.sharding import PartitionSpec as P


def neighbour_planes(fields, axis):
    count = lax.axis_size(axis)
    up = [(i, i + 1) for i in range(count - 1)]
    down = [(j, i) for i, j in up]
    below = lax.ppermute(jnp.concatenate([f[-1:] for f in fields]), axis, up)
    above = lax.ppermute(jnp.concatenate([f[:1] for f in fields]), axis, down)
    return below, above


def conv_valid(planes, kernel):
    out = lax.conv_general_dilated(
        planes[None],
        kernel,
        (1, 1, 1),
        "VALID",
        dimension_numbers=("NDHWC", "DHWIO", "NDHWC"),
        preferred_element_type=jnp.float32,
    )
    return out[0]


def pad_sides(field):
    return jnp.pad(field, ((0, 0), (1, 1), (1, 1), (0, 0)))


def conv_split(local, below, above, kernel):
    lo = conv_valid(local, kernel[1:3])[0] + conv_valid(below, kernel[0:1])[0]
    hi = conv_valid(local, kernel[0:2])[0] + conv_valid(above, kernel[2:3])[0]
    return jnp.stack((lo, hi)).astype(jnp.bfloat16)


def column_stack(padded):
    width = padded.shape[2] - 2
    return jnp.concatenate([padded[:, :, c:c + width, :] for c in range(3)], -1)


def weight_rows(local, halos, grads):
    height = grads.shape[1]
    xl = column_stack(local)
    xh = column_stack(halos)
    out = []
    for b in range(3):
        m = jnp.einsum("phwk,qhwo->pqko", xl[:, b:b + height], grads,
                       preferred_element_type=jnp.float32)
        mh = jnp.einsum("phwk,phwo->pko", xh[:, b:b + height], grads,
                        preferred_element_type=jnp.float32)
        out.append(jnp.stack((m[0, 1] + mh[0], m[0, 0] + m[1, 1], m[1, 0] + mh[1])))
    return jnp.stack(out, 1)


def stage_orders(bits):
    rest = list(range(1, bits))
    split = len(rest) // 2
    return [0] + rest, [0] + rest[split:] + rest[:split]


def halving_sum(x, axis):
    count = lax.axis_size(axis)
    me = lax.axis_index(axis)
    bits = count.bit_length() - 1
    assert 1 << bits == count
    order_a, order_b = stage_orders(bits)
    odd = me & 1
    shape = x.shape
    flat = x.reshape(-1, shape[-1])
    rows = flat.shape[0]
    unit = count * 8
    padded_rows = -(-rows // unit) * unit
    flat = jnp.pad(flat, ((0, padded_rows - rows), (0, 0)))
    def partner(i, step):
        k = order_b[step] if i & 1 else order_a[step]
        return i ^ (1 << k)
    def my_bit(step):
        return jnp.where(odd == 1, (me >> order_b[step]) & 1, (me >> order_a[step]) & 1)
    for step in range(bits):
        half = flat.shape[0] // 2
        bit = my_bit(step)
        keep = lax.dynamic_slice_in_dim(flat, bit * half, half, 0)
        send = lax.dynamic_slice_in_dim(flat, (1 - bit) * half, half, 0)
        pairs = [(i, partner(i, step)) for i in range(count)]
        flat = keep + lax.ppermute(send, axis, pairs)
    for step in reversed(range(bits)):
        bit = my_bit(step)
        pairs = [(i, partner(i, step)) for i in range(count)]
        other = lax.ppermute(flat, axis, pairs)
        low = jnp.where(bit == 0, flat, other)
        high = jnp.where(bit == 0, other, flat)
        flat = jnp.concatenate([low, high], 0)
    return flat[:rows].reshape(shape)


def body(volume, kernel, grad_out):
    assert volume.shape[0] == 2
    below, above = neighbour_planes((volume, grad_out), "slab")
    vol_p = pad_sides(volume)
    grad_p = pad_sides(grad_out)
    vol_below, vol_above = pad_sides(below[0:1]), pad_sides(above[0:1])
    cells = lax.axis_size("slab") * grad_out.shape[0] * grad_out.shape[1] * grad_out.shape[2]
    factor = 1.0 / jnp.sqrt(jnp.float32(cells))
    rows = weight_rows(vol_p, jnp.concatenate((vol_below, vol_above)), grad_out)
    terms = rows.reshape(3, 3, 3, kernel.shape[3], kernel.shape[4])
    weight_grad = halving_sum(terms, "slab") * factor
    grad_below, grad_above = pad_sides(below[1:2]), pad_sides(above[1:2])
    activation = conv_split(vol_p, vol_below, vol_above, kernel)
    flipped = jnp.swapaxes(kernel[::-1, ::-1, ::-1], 3, 4)
    input_grad = conv_split(grad_p, grad_below, grad_above, flipped)
    return (activation, input_grad, weight_grad)


def solution(mesh):
    return jax.shard_map(
        body,
        mesh=mesh,
        in_specs=(
            P(("groups", "slab"), None, None, None),
            P(),
            P(("groups", "slab"), None, None, None),
        ),
        out_specs=(
            P(("groups", "slab"), None, None, None),
            P(("groups", "slab"), None, None, None),
            P("groups", None, None, None, None),
        ),
        check_vma=False,
    )
```

```python
import jax
import jax.numpy as jnp
from jax import lax
from jax.sharding import PartitionSpec as P


def neighbour_planes(fields, axis):
    count = lax.axis_size(axis)
    up = [(i, i + 1) for i in range(count - 1)]
    down = [(j, i) for i, j in up]
    below = lax.ppermute(jnp.concatenate([f[-1:] for f in fields]), axis, up)
    above = lax.ppermute(jnp.concatenate([f[:1] for f in fields]), axis, down)
    return below, above


def conv_valid(planes, kernel):
    out = lax.conv_general_dilated(
        planes[None],
        kernel,
        (1, 1, 1),
        "VALID",
        dimension_numbers=("NDHWC", "DHWIO", "NDHWC"),
        preferred_element_type=jnp.float32,
    )
    return out[0]


def pad_sides(field):
    return jnp.pad(field, ((0, 0), (1, 1), (1, 1), (0, 0)))


def conv_split(local, below, above, kernel):
    lo = conv_valid(local, kernel[1:3])[0] + conv_valid(below, kernel[0:1])[0]
    hi = conv_valid(local, kernel[0:2])[0] + conv_valid(above, kernel[2:3])[0]
    return jnp.stack((lo, hi)).astype(jnp.bfloat16)


def column_stack(padded):
    width = padded.shape[2] - 2
    return jnp.concatenate([padded[:, :, c:c + width, :] for c in range(3)], -1)


def weight_rows(local, halos, grads):
    height = grads.shape[1]
    xl = column_stack(local)
    xh = column_stack(halos)
    centre, outer = [], []
    for b in range(3):
        m = jnp.einsum("phwk,qhwo->pqko", xl[:, b:b + height], grads,
                       preferred_element_type=jnp.float32)
        mh = jnp.einsum("phwk,phwo->pko", xh[:, b:b + height], grads,
                        preferred_element_type=jnp.float32)
        centre.append(m[0, 0] + m[1, 1])
        outer.append(jnp.stack((m[0, 1] + mh[0], m[1, 0] + mh[1])))
    return jnp.stack(centre), jnp.stack(outer)


def stage_orders(bits):
    rest = list(range(1, bits))
    split = len(rest) // 2
    return [0] + rest, [0] + rest[split:] + rest[:split]


def halving_sum(x, axis):
    count = lax.axis_size(axis)
    me = lax.axis_index(axis)
    bits = count.bit_length() - 1
    assert 1 << bits == count
    order_a, order_b = stage_orders(bits)
    odd = me & 1
    shape = x.shape
    flat = x.reshape(-1, shape[-1])
    rows = flat.shape[0]
    unit = count * 8
    padded_rows = -(-rows // unit) * unit
    flat = jnp.pad(flat, ((0, padded_rows - rows), (0, 0)))
    def partner(i, step):
        k = order_b[step] if i & 1 else order_a[step]
        return i ^ (1 << k)
    def my_bit(step):
        return jnp.where(odd == 1, (me >> order_b[step]) & 1, (me >> order_a[step]) & 1)
    for step in range(bits):
        half = flat.shape[0] // 2
        bit = my_bit(step)
        keep = lax.dynamic_slice_in_dim(flat, bit * half, half, 0)
        send = lax.dynamic_slice_in_dim(flat, (1 - bit) * half, half, 0)
        pairs = [(i, partner(i, step)) for i in range(count)]
        flat = keep + lax.ppermute(send, axis, pairs)
    for step in reversed(range(bits)):
        bit = my_bit(step)
        pairs = [(i, partner(i, step)) for i in range(count)]
        other = lax.ppermute(flat, axis, pairs)
        low = jnp.where(bit == 0, flat, other)
        high = jnp.where(bit == 0, other, flat)
        flat = jnp.concatenate([low, high], 0)
    return flat[:rows].reshape(shape)


def body(volume, kernel, grad_out):
    assert volume.shape[0] == 2
    below, above = neighbour_planes((volume, grad_out), "slab")
    vol_p = pad_sides(volume)
    grad_p = pad_sides(grad_out)
    vol_below, vol_above = pad_sides(below[0:1]), pad_sides(above[0:1])
    cells = lax.axis_size("slab") * grad_out.shape[0] * grad_out.shape[1] * grad_out.shape[2]
    factor = 1.0 / jnp.sqrt(jnp.float32(cells))
    centre, outer = weight_rows(vol_p, jnp.concatenate((vol_below, vol_above)), grad_out)
    centre = halving_sum(centre, "slab")
    outer = halving_sum(outer, "slab")
    taps = jnp.stack((outer[:, 0], centre, outer[:, 1]))
    weight_grad = taps.reshape(3, 3, 3, kernel.shape[3], kernel.shape[4]) * factor
    grad_below, grad_above = pad_sides(below[1:2]), pad_sides(above[1:2])
    activation = conv_split(vol_p, vol_below, vol_above, kernel)
    flipped = jnp.swapaxes(kernel[::-1, ::-1, ::-1], 3, 4)
    input_grad = conv_split(grad_p, grad_below, grad_above, flipped)
    return (activation, input_grad, weight_grad)


def solution(mesh):
    return jax.shard_map(
        body,
        mesh=mesh,
        in_specs=(
            P(("groups", "slab"), None, None, None),
            P(),
            P(("groups", "slab"), None, None, None),
        ),
        out_specs=(
            P(("groups", "slab"), None, None, None),
            P(("groups", "slab"), None, None, None),
            P("groups", None, None, None, None),
        ),
        check_vma=False,
    )
```

```python
import jax
import jax.numpy as jnp
from jax import lax
from jax.sharding import PartitionSpec as P


def neighbour_planes(fields, axis):
    count = lax.axis_size(axis)
    up = [(i, i + 1) for i in range(count - 1)]
    down = [(j, i) for i, j in up]
    below = lax.ppermute(jnp.concatenate([f[-1:] for f in fields]), axis, up)
    above = lax.ppermute(jnp.concatenate([f[:1] for f in fields]), axis, down)
    return below, above


def conv_valid(planes, kernel):
    out = lax.conv_general_dilated(
        planes[None],
        kernel,
        (1, 1, 1),
        "VALID",
        dimension_numbers=("NDHWC", "DHWIO", "NDHWC"),
        preferred_element_type=jnp.float32,
    )
    return out[0]


def pad_sides(field):
    return jnp.pad(field, ((0, 0), (1, 1), (1, 1), (0, 0)))


def conv_split(local, below, above, kernel):
    lo = conv_valid(local, kernel[1:3])[0] + conv_valid(below, kernel[0:1])[0]
    hi = conv_valid(local, kernel[0:2])[0] + conv_valid(above, kernel[2:3])[0]
    return jnp.stack((lo, hi)).astype(jnp.bfloat16)


def column_stack(padded):
    width = padded.shape[2] - 2
    return jnp.concatenate([padded[:, :, c:c + width, :] for c in range(3)], -1)


def weight_rows(local, halos, grads):
    height = grads.shape[1]
    xl = column_stack(local)
    xh = column_stack(halos)
    out = []
    for b in range(3):
        m = jnp.einsum("phwk,qhwo->pqko", xl[:, b:b + height], grads,
                       preferred_element_type=jnp.float32)
        mh = jnp.einsum("phwk,phwo->pko", xh[:, b:b + height], grads,
                        preferred_element_type=jnp.float32)
        out.append(jnp.stack((m[0, 1] + mh[0], m[0, 0] + m[1, 1], m[1, 0] + mh[1])))
    return jnp.stack(out, 1)


def stage_orders(bits):
    rest = list(range(1, bits))
    split = len(rest) // 2
    return [0] + rest, [0] + rest[split:] + rest[:split]


def halving_sum(x, axis):
    count = lax.axis_size(axis)
    me = lax.axis_index(axis)
    bits = count.bit_length() - 1
    assert 1 << bits == count
    order_a, order_b = stage_orders(bits)
    odd = me & 1
    shape = x.shape
    flat = x.reshape(-1, shape[-1])
    rows = flat.shape[0]
    unit = count * 8
    padded_rows = -(-rows // unit) * unit
    flat = jnp.pad(flat, ((0, padded_rows - rows), (0, 0)))
    def partner(i, step):
        k = order_b[step] if i & 1 else order_a[step]
        return i ^ (1 << k)
    def my_bit(step):
        return jnp.where(odd == 1, (me >> order_b[step]) & 1, (me >> order_a[step]) & 1)
    for step in range(bits):
        half = flat.shape[0] // 2
        bit = my_bit(step)
        keep = lax.dynamic_slice_in_dim(flat, bit * half, half, 0)
        send = lax.dynamic_slice_in_dim(flat, (1 - bit) * half, half, 0)
        pairs = [(i, partner(i, step)) for i in range(count)]
        flat = keep + lax.ppermute(send, axis, pairs)
    for step in reversed(range(bits)):
        bit = my_bit(step)
        pairs = [(i, partner(i, step)) for i in range(count)]
        other = lax.ppermute(flat, axis, pairs)
        low = jnp.where(bit == 0, flat, other)
        high = jnp.where(bit == 0, other, flat)
        flat = jnp.concatenate([low, high], 0)
    return flat[:rows].reshape(shape)


def body(volume, kernel, grad_out):
    assert volume.shape[0] == 2
    below, above = neighbour_planes((volume,), "slab")
    grad_below, grad_above = neighbour_planes((grad_out,), "slab")
    vol_p = pad_sides(volume)
    grad_p = pad_sides(grad_out)
    vol_below, vol_above = pad_sides(below), pad_sides(above)
    cells = lax.axis_size("slab") * grad_out.shape[0] * grad_out.shape[1] * grad_out.shape[2]
    factor = 1.0 / jnp.sqrt(jnp.float32(cells))
    rows = weight_rows(vol_p, jnp.concatenate((vol_below, vol_above)), grad_out)
    terms = rows.reshape(3, 3, 3, kernel.shape[3], kernel.shape[4])
    weight_grad = halving_sum(terms, "slab") * factor
    grad_below, grad_above = pad_sides(grad_below), pad_sides(grad_above)
    activation = conv_split(vol_p, vol_below, vol_above, kernel)
    flipped = jnp.swapaxes(kernel[::-1, ::-1, ::-1], 3, 4)
    input_grad = conv_split(grad_p, grad_below, grad_above, flipped)
    return (activation, input_grad, weight_grad)


def solution(mesh):
    return jax.shard_map(
        body,
        mesh=mesh,
        in_specs=(
            P(("groups", "slab"), None, None, None),
            P(),
            P(("groups", "slab"), None, None, None),
        ),
        out_specs=(
            P(("groups", "slab"), None, None, None),
            P(("groups", "slab"), None, None, None),
            P("groups", None, None, None, None),
        ),
        check_vma=False,
    )
```

```python
import jax
import jax.numpy as jnp
from jax import lax
from jax.sharding import PartitionSpec as P


def neighbour_planes(fields, axis):
    count = lax.axis_size(axis)
    up = [(i, i + 1) for i in range(count - 1)]
    down = [(j, i) for i, j in up]
    below = lax.ppermute(jnp.concatenate([f[-1:] for f in fields]), axis, up)
    above = lax.ppermute(jnp.concatenate([f[:1] for f in fields]), axis, down)
    return below, above


def conv_valid(planes, kernel):
    out = lax.conv_general_dilated(
        planes[None],
        kernel,
        (1, 1, 1),
        "VALID",
        dimension_numbers=("NDHWC", "DHWIO", "NDHWC"),
        preferred_element_type=jnp.float32,
    )
    return out[0]


def pad_sides(field):
    return jnp.pad(field, ((0, 0), (1, 1), (1, 1), (0, 0)))


def column_stack(padded):
    width = padded.shape[2] - 2
    return jnp.concatenate([padded[:, :, c:c + width, :] for c in range(3)], -1)


def weight_rows(local, halos, grads):
    height = grads.shape[1]
    xl = column_stack(local)
    xh = column_stack(halos)
    out = []
    for b in range(3):
        m = jnp.einsum("phwk,qhwo->pqko", xl[:, b:b + height], grads,
                       preferred_element_type=jnp.float32)
        mh = jnp.einsum("phwk,phwo->pko", xh[:, b:b + height], grads,
                        preferred_element_type=jnp.float32)
        out.append(jnp.stack((m[0, 1] + mh[0], m[0, 0] + m[1, 1], m[1, 0] + mh[1])))
    return jnp.stack(out, 1)


def stage_orders(bits):
    rest = list(range(1, bits))
    split = len(rest) // 2
    return [0] + rest, [0] + rest[split:] + rest[:split]


def halving_sum(x, axis):
    count = lax.axis_size(axis)
    me = lax.axis_index(axis)
    bits = count.bit_length() - 1
    assert 1 << bits == count
    order_a, order_b = stage_orders(bits)
    odd = me & 1
    shape = x.shape
    flat = x.reshape(-1, shape[-1])
    rows = flat.shape[0]
    unit = count * 8
    padded_rows = -(-rows // unit) * unit
    flat = jnp.pad(flat, ((0, padded_rows - rows), (0, 0)))
    def partner(i, step):
        k = order_b[step] if i & 1 else order_a[step]
        return i ^ (1 << k)
    def my_bit(step):
        return jnp.where(odd == 1, (me >> order_b[step]) & 1, (me >> order_a[step]) & 1)
    for step in range(bits):
        half = flat.shape[0] // 2
        bit = my_bit(step)
        keep = lax.dynamic_slice_in_dim(flat, bit * half, half, 0)
        send = lax.dynamic_slice_in_dim(flat, (1 - bit) * half, half, 0)
        pairs = [(i, partner(i, step)) for i in range(count)]
        flat = keep + lax.ppermute(send, axis, pairs)
    for step in reversed(range(bits)):
        bit = my_bit(step)
        pairs = [(i, partner(i, step)) for i in range(count)]
        other = lax.ppermute(flat, axis, pairs)
        low = jnp.where(bit == 0, flat, other)
        high = jnp.where(bit == 0, other, flat)
        flat = jnp.concatenate([low, high], 0)
    return flat[:rows].reshape(shape)


def body(volume, kernel, grad_out):
    assert volume.shape[0] == 2
    below, above = neighbour_planes((volume, grad_out), "slab")
    vol_p = pad_sides(volume)
    grad_p = pad_sides(grad_out)
    vol_below, vol_above = pad_sides(below[0:1]), pad_sides(above[0:1])
    cells = lax.axis_size("slab") * grad_out.shape[0] * grad_out.shape[1] * grad_out.shape[2]
    factor = 1.0 / jnp.sqrt(jnp.float32(cells))
    rows = weight_rows(vol_p, jnp.concatenate((vol_below, vol_above)), grad_out)
    terms = rows.reshape(3, 3, 3, kernel.shape[3], kernel.shape[4])
    weight_grad = halving_sum(terms, "slab") * factor
    grad_below, grad_above = pad_sides(below[1:2]), pad_sides(above[1:2])
    activation = conv_valid(jnp.concatenate((vol_below, vol_p, vol_above)), kernel)
    flipped = jnp.swapaxes(kernel[::-1, ::-1, ::-1], 3, 4)
    input_grad = conv_valid(jnp.concatenate((grad_below, grad_p, grad_above)), flipped)
    activation = activation.astype(jnp.bfloat16)
    input_grad = input_grad.astype(jnp.bfloat16)
    return (activation, input_grad, weight_grad)


def solution(mesh):
    return jax.shard_map(
        body,
        mesh=mesh,
        in_specs=(
            P(("groups", "slab"), None, None, None),
            P(),
            P(("groups", "slab"), None, None, None),
        ),
        out_specs=(
            P(("groups", "slab"), None, None, None),
            P(("groups", "slab"), None, None, None),
            P("groups", None, None, None, None),
        ),
        check_vma=False,
    )
```

```python
import jax
import jax.numpy as jnp
from jax import lax
from jax.sharding import PartitionSpec as P


def neighbour_planes(fields, axis):
    count = lax.axis_size(axis)
    up = [(i, i + 1) for i in range(count - 1)]
    down = [(j, i) for i, j in up]
    below = lax.ppermute(jnp.concatenate([f[-1:] for f in fields]), axis, up)
    above = lax.ppermute(jnp.concatenate([f[:1] for f in fields]), axis, down)
    return below, above


def conv_valid(planes, kernel):
    out = lax.conv_general_dilated(
        planes[None],
        kernel,
        (1, 1, 1),
        "VALID",
        dimension_numbers=("NDHWC", "DHWIO", "NDHWC"),
        preferred_element_type=jnp.float32,
    )
    return out[0]


def conv_by_plane(extended, kernel):
    planes = extended.shape[0] - 2
    out = [conv_valid(extended[d:d + 3], kernel)[0] for d in range(planes)]
    return jnp.stack(out).astype(jnp.bfloat16)


def pad_sides(field):
    return jnp.pad(field, ((0, 0), (1, 1), (1, 1), (0, 0)))


def column_stack(padded):
    width = padded.shape[2] - 2
    return jnp.concatenate([padded[:, :, c:c + width, :] for c in range(3)], -1)


def weight_rows(local, halos, grads):
    height = grads.shape[1]
    xl = column_stack(local)
    xh = column_stack(halos)
    out = []
    for b in range(3):
        m = jnp.einsum("phwk,qhwo->pqko", xl[:, b:b + height], grads,
                       preferred_element_type=jnp.float32)
        mh = jnp.einsum("phwk,phwo->pko", xh[:, b:b + height], grads,
                        preferred_element_type=jnp.float32)
        out.append(jnp.stack((m[0, 1] + mh[0], m[0, 0] + m[1, 1], m[1, 0] + mh[1])))
    return jnp.stack(out, 1)


def stage_orders(bits):
    rest = list(range(1, bits))
    split = len(rest) // 2
    return [0] + rest, [0] + rest[split:] + rest[:split]


def halving_sum(x, axis):
    count = lax.axis_size(axis)
    me = lax.axis_index(axis)
    bits = count.bit_length() - 1
    assert 1 << bits == count
    order_a, order_b = stage_orders(bits)
    odd = me & 1
    shape = x.shape
    flat = x.reshape(-1, shape[-1])
    rows = flat.shape[0]
    unit = count * 8
    padded_rows = -(-rows // unit) * unit
    flat = jnp.pad(flat, ((0, padded_rows - rows), (0, 0)))
    def partner(i, step):
        k = order_b[step] if i & 1 else order_a[step]
        return i ^ (1 << k)
    def my_bit(step):
        return jnp.where(odd == 1, (me >> order_b[step]) & 1, (me >> order_a[step]) & 1)
    for step in range(bits):
        half = flat.shape[0] // 2
        bit = my_bit(step)
        keep = lax.dynamic_slice_in_dim(flat, bit * half, half, 0)
        send = lax.dynamic_slice_in_dim(flat, (1 - bit) * half, half, 0)
        pairs = [(i, partner(i, step)) for i in range(count)]
        flat = keep + lax.ppermute(send, axis, pairs)
    for step in reversed(range(bits)):
        bit = my_bit(step)
        pairs = [(i, partner(i, step)) for i in range(count)]
        other = lax.ppermute(flat, axis, pairs)
        low = jnp.where(bit == 0, flat, other)
        high = jnp.where(bit == 0, other, flat)
        flat = jnp.concatenate([low, high], 0)
    return flat[:rows].reshape(shape)


def body(volume, kernel, grad_out):
    assert volume.shape[0] == 2
    below, above = neighbour_planes((volume, grad_out), "slab")
    vol_p = pad_sides(volume)
    grad_p = pad_sides(grad_out)
    vol_below, vol_above = pad_sides(below[0:1]), pad_sides(above[0:1])
    cells = lax.axis_size("slab") * grad_out.shape[0] * grad_out.shape[1] * grad_out.shape[2]
    factor = 1.0 / jnp.sqrt(jnp.float32(cells))
    rows = weight_rows(vol_p, jnp.concatenate((vol_below, vol_above)), grad_out)
    terms = rows.reshape(3, 3, 3, kernel.shape[3], kernel.shape[4])
    weight_grad = halving_sum(terms, "slab") * factor
    grad_below, grad_above = pad_sides(below[1:2]), pad_sides(above[1:2])
    activation = conv_by_plane(jnp.concatenate((vol_below, vol_p, vol_above)), kernel)
    flipped = jnp.swapaxes(kernel[::-1, ::-1, ::-1], 3, 4)
    input_grad = conv_by_plane(jnp.concatenate((grad_below, grad_p, grad_above)), flipped)
    return (activation, input_grad, weight_grad)


def solution(mesh):
    return jax.shard_map(
        body,
        mesh=mesh,
        in_specs=(
            P(("groups", "slab"), None, None, None),
            P(),
            P(("groups", "slab"), None, None, None),
        ),
        out_specs=(
            P(("groups", "slab"), None, None, None),
            P(("groups", "slab"), None, None, None),
            P("groups", None, None, None, None),
        ),
        check_vma=False,
    )
```

```python
import jax
import jax.numpy as jnp
from jax import lax
from jax.sharding import PartitionSpec as P


def neighbour_planes(fields, axis):
    count = lax.axis_size(axis)
    up = [(i, i + 1) for i in range(count - 1)]
    down = [(j, i) for i, j in up]
    below = lax.ppermute(jnp.concatenate([f[-1:] for f in fields]), axis, up)
    above = lax.ppermute(jnp.concatenate([f[:1] for f in fields]), axis, down)
    return below, above


def conv_valid(planes, kernel):
    out = lax.conv_general_dilated(
        planes[None],
        kernel,
        (1, 1, 1),
        "VALID",
        dimension_numbers=("NDHWC", "DHWIO", "NDHWC"),
        preferred_element_type=jnp.float32,
    )
    return out[0]


def pad_sides(field):
    return jnp.pad(field, ((0, 0), (1, 1), (1, 1), (0, 0)))


def column_stack(padded):
    width = padded.shape[2] - 2
    return jnp.concatenate([padded[:, :, c:c + width, :] for c in range(3)], -1)


def weight_rows(local, halos, grads):
    height = grads.shape[1]
    xl = column_stack(local)
    xh = column_stack(halos)
    out = []
    for b in range(3):
        m = jnp.einsum("phwk,qhwo->pqko", xl[:, b:b + height], grads,
                       preferred_element_type=jnp.float32)
        mh = jnp.einsum("phwk,phwo->pko", xh[:, b:b + height], grads,
                        preferred_element_type=jnp.float32)
        out.append(jnp.stack((m[0, 1] + mh[0], m[0, 0] + m[1, 1], m[1, 0] + mh[1])))
    return jnp.stack(out, 1)


def stage_orders(bits):
    rest = list(range(1, bits))
    split = len(rest) // 2
    return [0] + rest, [0] + rest[split:] + rest[:split]


def halving_sum(x, axis, hold):
    count = lax.axis_size(axis)
    me = lax.axis_index(axis)
    bits = count.bit_length() - 1
    assert 1 << bits == count
    order_a, order_b = stage_orders(bits)
    odd = me & 1
    shape = x.shape
    flat = x.reshape(-1, shape[-1])
    rows = flat.shape[0]
    unit = count * 8
    padded_rows = -(-rows // unit) * unit
    flat = jnp.pad(flat, ((0, padded_rows - rows), (0, 0)))
    def partner(i, step):
        k = order_b[step] if i & 1 else order_a[step]
        return i ^ (1 << k)
    def my_bit(step):
        return jnp.where(odd == 1, (me >> order_b[step]) & 1, (me >> order_a[step]) & 1)
    for step in range(bits):
        half = flat.shape[0] // 2
        bit = my_bit(step)
        keep = lax.dynamic_slice_in_dim(flat, bit * half, half, 0)
        send = lax.dynamic_slice_in_dim(flat, (1 - bit) * half, half, 0)
        if step == 0:
            send, hold = lax.optimization_barrier((send, hold))
        pairs = [(i, partner(i, step)) for i in range(count)]
        flat = keep + lax.ppermute(send, axis, pairs)
    for step in reversed(range(bits)):
        bit = my_bit(step)
        pairs = [(i, partner(i, step)) for i in range(count)]
        other = lax.ppermute(flat, axis, pairs)
        low = jnp.where(bit == 0, flat, other)
        high = jnp.where(bit == 0, other, flat)
        flat = jnp.concatenate([low, high], 0)
    return flat[:rows].reshape(shape), hold


def body(volume, kernel, grad_out):
    assert volume.shape[0] == 2
    below, above = neighbour_planes((volume, grad_out), "slab")
    vol_p = pad_sides(volume)
    grad_p = pad_sides(grad_out)
    vol_below, vol_above = pad_sides(below[0:1]), pad_sides(above[0:1])
    cells = lax.axis_size("slab") * grad_out.shape[0] * grad_out.shape[1] * grad_out.shape[2]
    factor = 1.0 / jnp.sqrt(jnp.float32(cells))
    rows = weight_rows(vol_p, jnp.concatenate((vol_below, vol_above)), grad_out)
    terms = rows.reshape(3, 3, 3, kernel.shape[3], kernel.shape[4])
    grad_below, grad_above = pad_sides(below[1:2]), pad_sides(above[1:2])
    activation = conv_valid(jnp.concatenate((vol_below, vol_p, vol_above)), kernel)
    flipped = jnp.swapaxes(kernel[::-1, ::-1, ::-1], 3, 4)
    input_grad = conv_valid(jnp.concatenate((grad_below, grad_p, grad_above)), flipped)
    activation = activation.astype(jnp.bfloat16)
    input_grad = input_grad.astype(jnp.bfloat16)
    summed, (activation, input_grad) = halving_sum(terms, "slab", (activation, input_grad))
    weight_grad = summed * factor
    return (activation, input_grad, weight_grad)


def solution(mesh):
    return jax.shard_map(
        body,
        mesh=mesh,
        in_specs=(
            P(("groups", "slab"), None, None, None),
            P(),
            P(("groups", "slab"), None, None, None),
        ),
        out_specs=(
            P(("groups", "slab"), None, None, None),
            P(("groups", "slab"), None, None, None),
            P("groups", None, None, None, None),
        ),
        check_vma=False,
    )
```

```python
import jax
import jax.numpy as jnp
from jax import lax
from jax.sharding import PartitionSpec as P


def neighbour_planes(fields, axis):
    count = lax.axis_size(axis)
    up = [(i, i + 1) for i in range(count - 1)]
    down = [(j, i) for i, j in up]
    below = lax.ppermute(jnp.concatenate([f[-1:] for f in fields]), axis, up)
    above = lax.ppermute(jnp.concatenate([f[:1] for f in fields]), axis, down)
    return below, above


def conv_valid(planes, kernel):
    out = lax.conv_general_dilated(
        planes[None],
        kernel,
        (1, 1, 1),
        "VALID",
        dimension_numbers=("NDHWC", "DHWIO", "NDHWC"),
        preferred_element_type=jnp.float32,
    )
    return out[0]


def pad_sides(field):
    return jnp.pad(field, ((0, 0), (1, 1), (1, 1), (0, 0)))


def column_stack(padded):
    width = padded.shape[2] - 2
    return jnp.concatenate([padded[:, :, c:c + width, :] for c in range(3)], -1)


def weight_rows(local, halos, grads):
    height = grads.shape[1]
    xl = column_stack(local)
    xh = column_stack(halos)
    out = []
    for b in range(3):
        m = jnp.einsum("phwk,qhwo->pqko", xl[:, b:b + height], grads,
                       preferred_element_type=jnp.float32)
        mh = jnp.einsum("phwk,phwo->pko", xh[:, b:b + height], grads,
                        preferred_element_type=jnp.float32)
        out.append(jnp.stack((m[0, 1] + mh[0], m[0, 0] + m[1, 1], m[1, 0] + mh[1])))
    return jnp.stack(out, 1)


def stage_groups(bits):
    rest = list(range(1, bits))
    groups = [[0]]
    if len(rest) % 2:
        groups.append([rest.pop(0)])
    groups += [rest[j:j + 2] for j in range(0, len(rest), 2)]
    return groups


def halving_sum(x, axis):
    count = lax.axis_size(axis)
    me = lax.axis_index(axis)
    bits = count.bit_length() - 1
    assert 1 << bits == count
    groups = stage_groups(bits)
    shape = x.shape
    flat = x.reshape(-1, shape[-1])
    rows = flat.shape[0]
    unit = count * 8
    padded_rows = -(-rows // unit) * unit
    flat = jnp.pad(flat, ((0, padded_rows - rows), (0, 0)))

    def mask(group, t):
        return sum(((t >> j) & 1) << b for j, b in enumerate(group))

    def slot(group):
        return sum(((me >> b) & 1) << j for j, b in enumerate(group))

    for group in groups:
        size = 1 << len(group)
        part = flat.shape[0] // size
        mine = slot(group)
        total = lax.dynamic_slice_in_dim(flat, mine * part, part, 0)
        for t in range(1, size):
            send = lax.dynamic_slice_in_dim(flat, (mine ^ t) * part, part, 0)
            pairs = [(i, i ^ mask(group, t)) for i in range(count)]
            total = total + lax.ppermute(send, axis, pairs)
        flat = total
    for group in reversed(groups):
        size = 1 << len(group)
        mine = slot(group)
        got = [flat] + [lax.ppermute(flat, axis, [(i, i ^ mask(group, t)) for i in range(count)])
                        for t in range(1, size)]
        blocks = []
        for j in range(size):
            block = got[0]
            for t in range(1, size):
                block = jnp.where((mine ^ t) == j, got[t], block)
            blocks.append(block)
        flat = jnp.concatenate(blocks, 0)
    return flat[:rows].reshape(shape)


def body(volume, kernel, grad_out):
    assert volume.shape[0] == 2
    below, above = neighbour_planes((volume, grad_out), "slab")
    vol_p = pad_sides(volume)
    grad_p = pad_sides(grad_out)
    vol_below, vol_above = pad_sides(below[0:1]), pad_sides(above[0:1])
    cells = lax.axis_size("slab") * grad_out.shape[0] * grad_out.shape[1] * grad_out.shape[2]
    factor = 1.0 / jnp.sqrt(jnp.float32(cells))
    rows = weight_rows(vol_p, jnp.concatenate((vol_below, vol_above)), grad_out)
    terms = rows.reshape(3, 3, 3, kernel.shape[3], kernel.shape[4])
    weight_grad = halving_sum(terms, "slab") * factor
    grad_below, grad_above = pad_sides(below[1:2]), pad_sides(above[1:2])
    activation = conv_valid(jnp.concatenate((vol_below, vol_p, vol_above)), kernel)
    flipped = jnp.swapaxes(kernel[::-1, ::-1, ::-1], 3, 4)
    input_grad = conv_valid(jnp.concatenate((grad_below, grad_p, grad_above)), flipped)
    activation = activation.astype(jnp.bfloat16)
    input_grad = input_grad.astype(jnp.bfloat16)
    return (activation, input_grad, weight_grad)


def solution(mesh):
    return jax.shard_map(
        body,
        mesh=mesh,
        in_specs=(
            P(("groups", "slab"), None, None, None),
            P(),
            P(("groups", "slab"), None, None, None),
        ),
        out_specs=(
            P(("groups", "slab"), None, None, None),
            P(("groups", "slab"), None, None, None),
            P("groups", None, None, None, None),
        ),
        check_vma=False,
    )
```

```python
import jax
import jax.numpy as jnp
from jax import lax
from jax.sharding import PartitionSpec as P


def neighbour_planes(fields, axis):
    count = lax.axis_size(axis)
    up = [(i, i + 1) for i in range(count - 1)]
    down = [(j, i) for i, j in up]
    below = lax.ppermute(jnp.concatenate([f[-1:] for f in fields]), axis, up)
    above = lax.ppermute(jnp.concatenate([f[:1] for f in fields]), axis, down)
    return below, above


def conv_valid(planes, kernel):
    out = lax.conv_general_dilated(
        planes[None],
        kernel,
        (1, 1, 1),
        "VALID",
        dimension_numbers=("NDHWC", "DHWIO", "NDHWC"),
        preferred_element_type=jnp.float32,
    )
    return out[0]


def pad_sides(field):
    return jnp.pad(field, ((0, 0), (1, 1), (1, 1), (0, 0)))


def column_stack(padded):
    width = padded.shape[2] - 2
    return jnp.concatenate([padded[:, :, c:c + width, :] for c in range(3)], -1)


def weight_rows(local, halos, grads):
    height = grads.shape[1]
    xl = column_stack(local)
    xh = column_stack(halos)
    out = []
    for b in range(3):
        m = jnp.einsum("phwk,qhwo->pqko", xl[:, b:b + height], grads,
                       preferred_element_type=jnp.float32)
        mh = jnp.einsum("phwk,phwo->pko", xh[:, b:b + height], grads,
                        preferred_element_type=jnp.float32)
        out.append(jnp.stack((m[0, 1] + mh[0], m[0, 0] + m[1, 1], m[1, 0] + mh[1])))
    return jnp.stack(out, 1)


def stage_groups(bits):
    rest = list(range(1, bits))
    groups = [[0]]
    if len(rest) % 2:
        groups.append([rest.pop(0)])
    groups += [rest[j:j + 2] for j in range(0, len(rest), 2)]
    return groups


def halving_sum(x, axis, hold):
    count = lax.axis_size(axis)
    me = lax.axis_index(axis)
    bits = count.bit_length() - 1
    assert 1 << bits == count
    groups = stage_groups(bits)
    shape = x.shape
    flat = x.reshape(-1, shape[-1])
    rows = flat.shape[0]
    unit = count * 8
    padded_rows = -(-rows // unit) * unit
    flat = jnp.pad(flat, ((0, padded_rows - rows), (0, 0)))

    def mask(group, t):
        return sum(((t >> j) & 1) << b for j, b in enumerate(group))

    def slot(group):
        return sum(((me >> b) & 1) << j for j, b in enumerate(group))

    for group in groups:
        size = 1 << len(group)
        part = flat.shape[0] // size
        mine = slot(group)
        total = lax.dynamic_slice_in_dim(flat, mine * part, part, 0)
        for t in range(1, size):
            send = lax.dynamic_slice_in_dim(flat, (mine ^ t) * part, part, 0)
            pairs = [(i, i ^ mask(group, t)) for i in range(count)]
            total = total + lax.ppermute(send, axis, pairs)
        flat = total
    for group in reversed(groups):
        if group is groups[0]:
            flat, hold = lax.optimization_barrier((flat, hold))
        size = 1 << len(group)
        mine = slot(group)
        got = [flat] + [lax.ppermute(flat, axis, [(i, i ^ mask(group, t)) for i in range(count)])
                        for t in range(1, size)]
        blocks = []
        for j in range(size):
            block = got[0]
            for t in range(1, size):
                block = jnp.where((mine ^ t) == j, got[t], block)
            blocks.append(block)
        flat = jnp.concatenate(blocks, 0)
    return flat[:rows].reshape(shape), hold


def body(volume, kernel, grad_out):
    assert volume.shape[0] == 2
    below, above = neighbour_planes((volume, grad_out), "slab")
    vol_p = pad_sides(volume)
    grad_p = pad_sides(grad_out)
    vol_below, vol_above = pad_sides(below[0:1]), pad_sides(above[0:1])
    cells = lax.axis_size("slab") * grad_out.shape[0] * grad_out.shape[1] * grad_out.shape[2]
    factor = 1.0 / jnp.sqrt(jnp.float32(cells))
    rows = weight_rows(vol_p, jnp.concatenate((vol_below, vol_above)), grad_out)
    terms = rows.reshape(3, 3, 3, kernel.shape[3], kernel.shape[4])
    grad_below, grad_above = pad_sides(below[1:2]), pad_sides(above[1:2])
    activation = conv_valid(jnp.concatenate((vol_below, vol_p, vol_above)), kernel)
    flipped = jnp.swapaxes(kernel[::-1, ::-1, ::-1], 3, 4)
    input_grad = conv_valid(jnp.concatenate((grad_below, grad_p, grad_above)), flipped)
    activation = activation.astype(jnp.bfloat16)
    input_grad = input_grad.astype(jnp.bfloat16)
    summed, (activation, input_grad) = halving_sum(terms, "slab", (activation, input_grad))
    weight_grad = summed * factor
    return (activation, input_grad, weight_grad)


def solution(mesh):
    return jax.shard_map(
        body,
        mesh=mesh,
        in_specs=(
            P(("groups", "slab"), None, None, None),
            P(),
            P(("groups", "slab"), None, None, None),
        ),
        out_specs=(
            P(("groups", "slab"), None, None, None),
            P(("groups", "slab"), None, None, None),
            P("groups", None, None, None, None),
        ),
        check_vma=False,
    )
```

```python
import jax
import jax.numpy as jnp
from jax import lax
from jax.sharding import PartitionSpec as P


def neighbour_planes(fields, axis):
    count = lax.axis_size(axis)
    up = [(i, i + 1) for i in range(count - 1)]
    down = [(j, i) for i, j in up]
    below = lax.ppermute(jnp.concatenate([f[-1:] for f in fields]), axis, up)
    above = lax.ppermute(jnp.concatenate([f[:1] for f in fields]), axis, down)
    return below, above


def conv_valid(planes, kernel):
    out = lax.conv_general_dilated(
        planes[None],
        kernel,
        (1, 1, 1),
        "VALID",
        dimension_numbers=("NDHWC", "DHWIO", "NDHWC"),
        preferred_element_type=jnp.float32,
    )
    return out[0]


def pad_sides(field):
    return jnp.pad(field, ((0, 0), (1, 1), (1, 1), (0, 0)))


def column_stack(padded):
    width = padded.shape[2] - 2
    return jnp.concatenate([padded[:, :, c:c + width, :] for c in range(3)], -1)


def weight_rows(local, halos, grads):
    height = grads.shape[1]
    xl = column_stack(local)
    xh = column_stack(halos)
    out = []
    for b in range(3):
        m = jnp.einsum("phwk,qhwo->pqko", xl[:, b:b + height], grads,
                       preferred_element_type=jnp.float32)
        mh = jnp.einsum("phwk,phwo->pko", xh[:, b:b + height], grads,
                        preferred_element_type=jnp.float32)
        out.append(jnp.stack((m[0, 1] + mh[0], m[0, 0] + m[1, 1], m[1, 0] + mh[1])))
    return jnp.stack(out, 1)


def stage_groups(bits):
    rest = list(range(1, bits))
    groups = [[0]]
    if len(rest) % 2:
        groups.append([rest.pop(0)])
    groups += [rest[j:j + 2] for j in range(0, len(rest), 2)]
    return groups


def halving_sum(x, axis, hold, late, late_fn):
    count = lax.axis_size(axis)
    me = lax.axis_index(axis)
    bits = count.bit_length() - 1
    assert 1 << bits == count
    groups = stage_groups(bits)
    shape = x.shape
    flat = x.reshape(-1, shape[-1])
    rows = flat.shape[0]
    unit = count * 8
    padded_rows = -(-rows // unit) * unit
    flat = jnp.pad(flat, ((0, padded_rows - rows), (0, 0)))

    def mask(group, t):
        return sum(((t >> j) & 1) << b for j, b in enumerate(group))

    def slot(group):
        return sum(((me >> b) & 1) << j for j, b in enumerate(group))

    for group in groups:
        size = 1 << len(group)
        part = flat.shape[0] // size
        mine = slot(group)
        total = lax.dynamic_slice_in_dim(flat, mine * part, part, 0)
        for t in range(1, size):
            send = lax.dynamic_slice_in_dim(flat, (mine ^ t) * part, part, 0)
            pairs = [(i, i ^ mask(group, t)) for i in range(count)]
            total = total + lax.ppermute(send, axis, pairs)
        flat = total
    for group in reversed(groups):
        if group is groups[1]:
            flat, late = lax.optimization_barrier((flat, late))
            hold = hold + (late_fn(late),)
        if group is groups[0]:
            flat, hold = lax.optimization_barrier((flat, hold))
        size = 1 << len(group)
        mine = slot(group)
        got = [flat] + [lax.ppermute(flat, axis, [(i, i ^ mask(group, t)) for i in range(count)])
                        for t in range(1, size)]
        blocks = []
        for j in range(size):
            block = got[0]
            for t in range(1, size):
                block = jnp.where((mine ^ t) == j, got[t], block)
            blocks.append(block)
        flat = jnp.concatenate(blocks, 0)
    return flat[:rows].reshape(shape), hold


def body(volume, kernel, grad_out):
    assert volume.shape[0] == 2
    below, above = neighbour_planes((volume, grad_out), "slab")
    vol_p = pad_sides(volume)
    grad_p = pad_sides(grad_out)
    vol_below, vol_above = pad_sides(below[0:1]), pad_sides(above[0:1])
    cells = lax.axis_size("slab") * grad_out.shape[0] * grad_out.shape[1] * grad_out.shape[2]
    factor = 1.0 / jnp.sqrt(jnp.float32(cells))
    rows = weight_rows(vol_p, jnp.concatenate((vol_below, vol_above)), grad_out)
    terms = rows.reshape(3, 3, 3, kernel.shape[3], kernel.shape[4])
    grad_below, grad_above = pad_sides(below[1:2]), pad_sides(above[1:2])
    activation = conv_valid(jnp.concatenate((vol_below, vol_p, vol_above)), kernel)
    activation = activation.astype(jnp.bfloat16)
    flipped = jnp.swapaxes(kernel[::-1, ::-1, ::-1], 3, 4)
    grad_ext = jnp.concatenate((grad_below, grad_p, grad_above))

    def late_conv(field):
        return conv_valid(field, flipped).astype(jnp.bfloat16)

    summed, (activation, input_grad) = halving_sum(
        terms, "slab", (activation,), grad_ext, late_conv)
    weight_grad = summed * factor
    return (activation, input_grad, weight_grad)


def solution(mesh):
    return jax.shard_map(
        body,
        mesh=mesh,
        in_specs=(
            P(("groups", "slab"), None, None, None),
            P(),
            P(("groups", "slab"), None, None, None),
        ),
        out_specs=(
            P(("groups", "slab"), None, None, None),
            P(("groups", "slab"), None, None, None),
            P("groups", None, None, None, None),
        ),
        check_vma=False,
    )
```

```python
import jax
import jax.numpy as jnp
from jax import lax
from jax.sharding import PartitionSpec as P


def neighbour_planes(fields, axis, after=()):
    count = lax.axis_size(axis)
    up = [(i, i + 1) for i in range(count - 1)]
    down = [(j, i) for i, j in up]
    last = jnp.concatenate([f[-1:] for f in fields])
    first = jnp.concatenate([f[:1] for f in fields])
    if after:
        last, first, _ = lax.optimization_barrier((last, first, after))
    below = lax.ppermute(last, axis, up)
    above = lax.ppermute(first, axis, down)
    return below, above


def conv_valid(planes, kernel):
    out = lax.conv_general_dilated(
        planes[None],
        kernel,
        (1, 1, 1),
        "VALID",
        dimension_numbers=("NDHWC", "DHWIO", "NDHWC"),
        preferred_element_type=jnp.float32,
    )
    return out[0]


def pad_sides(field):
    return jnp.pad(field, ((0, 0), (1, 1), (1, 1), (0, 0)))


def column_stack(padded):
    width = padded.shape[2] - 2
    return jnp.concatenate([padded[:, :, c:c + width, :] for c in range(3)], -1)


def weight_rows(local, halos, grads):
    height = grads.shape[1]
    xl = column_stack(local)
    xh = column_stack(halos)
    out = []
    for b in range(3):
        m = jnp.einsum("phwk,qhwo->pqko", xl[:, b:b + height], grads,
                       preferred_element_type=jnp.float32)
        mh = jnp.einsum("phwk,phwo->pko", xh[:, b:b + height], grads,
                        preferred_element_type=jnp.float32)
        out.append(jnp.stack((m[0, 1] + mh[0], m[0, 0] + m[1, 1], m[1, 0] + mh[1])))
    return jnp.stack(out, 1)


def stage_groups(bits):
    rest = list(range(1, bits))
    groups = [[0]]
    if len(rest) % 2:
        groups.append([rest.pop(0)])
    groups += [rest[j:j + 2] for j in range(0, len(rest), 2)]
    return groups


def halving_sum(x, axis, hold, late, late_fn):
    count = lax.axis_size(axis)
    me = lax.axis_index(axis)
    bits = count.bit_length() - 1
    assert 1 << bits == count
    groups = stage_groups(bits)
    shape = x.shape
    flat = x.reshape(-1, shape[-1])
    rows = flat.shape[0]
    unit = count * 8
    padded_rows = -(-rows // unit) * unit
    flat = jnp.pad(flat, ((0, padded_rows - rows), (0, 0)))

    def mask(group, t):
        return sum(((t >> j) & 1) << b for j, b in enumerate(group))

    def slot(group):
        return sum(((me >> b) & 1) << j for j, b in enumerate(group))

    for group in groups:
        size = 1 << len(group)
        part = flat.shape[0] // size
        mine = slot(group)
        total = lax.dynamic_slice_in_dim(flat, mine * part, part, 0)
        for t in range(1, size):
            send = lax.dynamic_slice_in_dim(flat, (mine ^ t) * part, part, 0)
            pairs = [(i, i ^ mask(group, t)) for i in range(count)]
            total = total + lax.ppermute(send, axis, pairs)
        flat = total
    for group in reversed(groups):
        if group is groups[1]:
            flat, late = lax.optimization_barrier((flat, late))
            hold = hold + (late_fn(late),)
        if group is groups[0]:
            flat, hold = lax.optimization_barrier((flat, hold))
        size = 1 << len(group)
        mine = slot(group)
        got = [flat] + [lax.ppermute(flat, axis, [(i, i ^ mask(group, t)) for i in range(count)])
                        for t in range(1, size)]
        blocks = []
        for j in range(size):
            block = got[0]
            for t in range(1, size):
                block = jnp.where((mine ^ t) == j, got[t], block)
            blocks.append(block)
        flat = jnp.concatenate(blocks, 0)
    return flat[:rows].reshape(shape), hold


def body(volume, kernel, grad_out):
    assert volume.shape[0] == 2
    below, above = neighbour_planes((volume,), "slab")
    grad_below, grad_above = neighbour_planes((grad_out,), "slab", (below, above))
    vol_p = pad_sides(volume)
    grad_p = pad_sides(grad_out)
    vol_below, vol_above = pad_sides(below), pad_sides(above)
    cells = lax.axis_size("slab") * grad_out.shape[0] * grad_out.shape[1] * grad_out.shape[2]
    factor = 1.0 / jnp.sqrt(jnp.float32(cells))
    rows = weight_rows(vol_p, jnp.concatenate((vol_below, vol_above)), grad_out)
    terms = rows.reshape(3, 3, 3, kernel.shape[3], kernel.shape[4])
    grad_below, grad_above = pad_sides(grad_below), pad_sides(grad_above)
    activation = conv_valid(jnp.concatenate((vol_below, vol_p, vol_above)), kernel)
    activation = activation.astype(jnp.bfloat16)
    flipped = jnp.swapaxes(kernel[::-1, ::-1, ::-1], 3, 4)
    grad_ext = jnp.concatenate((grad_below, grad_p, grad_above))

    def late_conv(field):
        return conv_valid(field, flipped).astype(jnp.bfloat16)

    summed, (activation, input_grad) = halving_sum(
        terms, "slab", (activation,), grad_ext, late_conv)
    weight_grad = summed * factor
    return (activation, input_grad, weight_grad)


def solution(mesh):
    return jax.shard_map(
        body,
        mesh=mesh,
        in_specs=(
            P(("groups", "slab"), None, None, None),
            P(),
            P(("groups", "slab"), None, None, None),
        ),
        out_specs=(
            P(("groups", "slab"), None, None, None),
            P(("groups", "slab"), None, None, None),
            P("groups", None, None, None, None),
        ),
        check_vma=False,
    )
```

```python
import jax
import jax.numpy as jnp
from jax import lax
from jax.sharding import PartitionSpec as P


def neighbour_planes(fields, axis):
    count = lax.axis_size(axis)
    up = [(i, i + 1) for i in range(count - 1)]
    down = [(j, i) for i, j in up]
    below = lax.ppermute(jnp.concatenate([f[-1:] for f in fields]), axis, up)
    above = lax.ppermute(jnp.concatenate([f[:1] for f in fields]), axis, down)
    return below, above


def conv_valid(planes, kernel):
    out = lax.conv_general_dilated(
        planes[None],
        kernel,
        (1, 1, 1),
        "VALID",
        dimension_numbers=("NDHWC", "DHWIO", "NDHWC"),
        preferred_element_type=jnp.float32,
    )
    return out[0]


def pad_sides(field):
    return jnp.pad(field, ((0, 0), (1, 1), (1, 1), (0, 0)))


def column_stack(padded):
    width = padded.shape[2] - 2
    return jnp.concatenate([padded[:, :, c:c + width, :] for c in range(3)], -1)


def conv_columns(extended, kernel):
    folded = kernel.reshape(3, 3, 1, 3 * kernel.shape[3], kernel.shape[4])
    return conv_valid(column_stack(extended), folded)


def weight_rows(local, halos, grads):
    height = grads.shape[1]
    xl = column_stack(local)
    xh = column_stack(halos)
    out = []
    for b in range(3):
        m = jnp.einsum("phwk,qhwo->pqko", xl[:, b:b + height], grads,
                       preferred_element_type=jnp.float32)
        mh = jnp.einsum("phwk,phwo->pko", xh[:, b:b + height], grads,
                        preferred_element_type=jnp.float32)
        out.append(jnp.stack((m[0, 1] + mh[0], m[0, 0] + m[1, 1], m[1, 0] + mh[1])))
    return jnp.stack(out, 1)


def stage_groups(bits):
    rest = list(range(1, bits))
    groups = [[0]]
    if len(rest) % 2:
        groups.append([rest.pop(0)])
    groups += [rest[j:j + 2] for j in range(0, len(rest), 2)]
    return groups


def halving_sum(x, axis, hold):
    count = lax.axis_size(axis)
    me = lax.axis_index(axis)
    bits = count.bit_length() - 1
    assert 1 << bits == count
    groups = stage_groups(bits)
    shape = x.shape
    flat = x.reshape(-1, shape[-1])
    rows = flat.shape[0]
    unit = count * 8
    padded_rows = -(-rows // unit) * unit
    flat = jnp.pad(flat, ((0, padded_rows - rows), (0, 0)))

    def mask(group, t):
        return sum(((t >> j) & 1) << b for j, b in enumerate(group))

    def slot(group):
        return sum(((me >> b) & 1) << j for j, b in enumerate(group))

    for group in groups:
        size = 1 << len(group)
        part = flat.shape[0] // size
        mine = slot(group)
        total = lax.dynamic_slice_in_dim(flat, mine * part, part, 0)
        for t in range(1, size):
            send = lax.dynamic_slice_in_dim(flat, (mine ^ t) * part, part, 0)
            pairs = [(i, i ^ mask(group, t)) for i in range(count)]
            total = total + lax.ppermute(send, axis, pairs)
        flat = total
    for group in reversed(groups):
        if group is groups[0]:
            flat, hold = lax.optimization_barrier((flat, hold))
        size = 1 << len(group)
        mine = slot(group)
        got = [flat] + [lax.ppermute(flat, axis, [(i, i ^ mask(group, t)) for i in range(count)])
                        for t in range(1, size)]
        blocks = []
        for j in range(size):
            block = got[0]
            for t in range(1, size):
                block = jnp.where((mine ^ t) == j, got[t], block)
            blocks.append(block)
        flat = jnp.concatenate(blocks, 0)
    return flat[:rows].reshape(shape), hold


def body(volume, kernel, grad_out):
    assert volume.shape[0] == 2
    below, above = neighbour_planes((volume, grad_out), "slab")
    vol_p = pad_sides(volume)
    grad_p = pad_sides(grad_out)
    vol_below, vol_above = pad_sides(below[0:1]), pad_sides(above[0:1])
    cells = lax.axis_size("slab") * grad_out.shape[0] * grad_out.shape[1] * grad_out.shape[2]
    factor = 1.0 / jnp.sqrt(jnp.float32(cells))
    rows = weight_rows(vol_p, jnp.concatenate((vol_below, vol_above)), grad_out)
    terms = rows.reshape(3, 3, 3, kernel.shape[3], kernel.shape[4])
    grad_below, grad_above = pad_sides(below[1:2]), pad_sides(above[1:2])
    activation = conv_columns(jnp.concatenate((vol_below, vol_p, vol_above)), kernel)
    flipped = jnp.swapaxes(kernel[::-1, ::-1, ::-1], 3, 4)
    input_grad = conv_columns(jnp.concatenate((grad_below, grad_p, grad_above)), flipped)
    activation = activation.astype(jnp.bfloat16)
    input_grad = input_grad.astype(jnp.bfloat16)
    summed, (activation, input_grad) = halving_sum(terms, "slab", (activation, input_grad))
    weight_grad = summed * factor
    return (activation, input_grad, weight_grad)


def solution(mesh):
    return jax.shard_map(
        body,
        mesh=mesh,
        in_specs=(
            P(("groups", "slab"), None, None, None),
            P(),
            P(("groups", "slab"), None, None, None),
        ),
        out_specs=(
            P(("groups", "slab"), None, None, None),
            P(("groups", "slab"), None, None, None),
            P("groups", None, None, None, None),
        ),
        check_vma=False,
    )
```

```python
import jax
import jax.numpy as jnp
from jax import lax
from jax.sharding import PartitionSpec as P


def neighbour_planes(fields, axis):
    count = lax.axis_size(axis)
    up = [(i, i + 1) for i in range(count - 1)]
    down = [(j, i) for i, j in up]
    below = lax.ppermute(jnp.concatenate([f[-1:] for f in fields]), axis, up)
    above = lax.ppermute(jnp.concatenate([f[:1] for f in fields]), axis, down)
    return below, above


def conv_valid(planes, kernel):
    out = lax.conv_general_dilated(
        planes[None],
        kernel,
        (1, 1, 1),
        "VALID",
        dimension_numbers=("NDHWC", "DHWIO", "NDHWC"),
        preferred_element_type=jnp.float32,
    )
    return out[0]


def pad_sides(field):
    return jnp.pad(field, ((0, 0), (1, 1), (1, 1), (0, 0)))


def column_stack(padded):
    width = padded.shape[2] - 2
    return jnp.concatenate([padded[:, :, c:c + width, :] for c in range(3)], -1)


def weight_rows(local, halos, grads):
    height = grads.shape[1]
    xl = column_stack(local)
    xh = column_stack(halos)
    out = []
    for b in range(3):
        m = jnp.einsum("phwk,qhwo->pqko", xl[:, b:b + height], grads,
                       preferred_element_type=jnp.float32)
        mh = jnp.einsum("phwk,phwo->pko", xh[:, b:b + height], grads,
                        preferred_element_type=jnp.float32)
        out.append(jnp.stack((m[0, 1] + mh[0], m[0, 0] + m[1, 1], m[1, 0] + mh[1])))
    return jnp.stack(out, 1)


def stage_groups(bits):
    rest = list(range(1, bits))
    groups = [[0]]
    if len(rest) % 2:
        groups.append([rest.pop(0)])
    groups += [rest[j:j + 2] for j in range(0, len(rest), 2)]
    return groups


def halving_sum(x, axis, hold):
    count = lax.axis_size(axis)
    me = lax.axis_index(axis)
    bits = count.bit_length() - 1
    assert 1 << bits == count
    groups = stage_groups(bits)
    shape = x.shape
    flat = x.reshape(-1, shape[-1])
    rows = flat.shape[0]
    unit = count * 8
    padded_rows = -(-rows // unit) * unit
    flat = jnp.pad(flat, ((0, padded_rows - rows), (0, 0)))

    def mask(group, t):
        return sum(((t >> j) & 1) << b for j, b in enumerate(group))

    def slot(group):
        return sum(((me >> b) & 1) << j for j, b in enumerate(group))

    for group in groups:
        size = 1 << len(group)
        part = flat.shape[0] // size
        mine = slot(group)
        total = lax.dynamic_slice_in_dim(flat, mine * part, part, 0)
        for t in range(1, size):
            send = lax.dynamic_slice_in_dim(flat, (mine ^ t) * part, part, 0)
            pairs = [(i, i ^ mask(group, t)) for i in range(count)]
            total = total + lax.ppermute(send, axis, pairs)
        flat = total
    for group in reversed(groups):
        if group is groups[0]:
            flat, hold = lax.optimization_barrier((flat, hold))
        size = 1 << len(group)
        mine = slot(group)
        got = [flat] + [lax.ppermute(flat, axis, [(i, i ^ mask(group, t)) for i in range(count)])
                        for t in range(1, size)]
        blocks = []
        for j in range(size):
            block = got[0]
            for t in range(1, size):
                block = jnp.where((mine ^ t) == j, got[t], block)
            blocks.append(block)
        flat = jnp.concatenate(blocks, 0)
    return flat[:rows].reshape(shape), hold


def body(volume, kernel, grad_out):
    assert volume.shape[0] == 2
    below, above = neighbour_planes((volume, grad_out), "slab")
    vol_p = pad_sides(volume)
    grad_p = pad_sides(grad_out)
    vol_below, vol_above = pad_sides(below[0:1]), pad_sides(above[0:1])
    cells = lax.axis_size("slab") * grad_out.shape[0] * grad_out.shape[1] * grad_out.shape[2]
    factor = 1.0 / jnp.sqrt(jnp.float32(cells))
    rows = weight_rows(vol_p, jnp.concatenate((vol_below, vol_above)), grad_out)
    terms = rows.reshape(3, 3, 3, kernel.shape[3], kernel.shape[4]) * factor
    grad_below, grad_above = pad_sides(below[1:2]), pad_sides(above[1:2])
    activation = conv_valid(jnp.concatenate((vol_below, vol_p, vol_above)), kernel)
    flipped = jnp.swapaxes(kernel[::-1, ::-1, ::-1], 3, 4)
    input_grad = conv_valid(jnp.concatenate((grad_below, grad_p, grad_above)), flipped)
    activation = activation.astype(jnp.bfloat16)
    input_grad = input_grad.astype(jnp.bfloat16)
    weight_grad, (activation, input_grad) = halving_sum(terms, "slab", (activation, input_grad))
    return (activation, input_grad, weight_grad)


def solution(mesh):
    return jax.shard_map(
        body,
        mesh=mesh,
        in_specs=(
            P(("groups", "slab"), None, None, None),
            P(),
            P(("groups", "slab"), None, None, None),
        ),
        out_specs=(
            P(("groups", "slab"), None, None, None),
            P(("groups", "slab"), None, None, None),
            P("groups", None, None, None, None),
        ),
        check_vma=False,
    )
```

```python
import jax
import jax.numpy as jnp
from jax import lax
from jax.sharding import PartitionSpec as P


def neighbour_planes(fields, axis):
    count = lax.axis_size(axis)
    up = [(i, i + 1) for i in range(count - 1)]
    down = [(j, i) for i, j in up]
    below = lax.ppermute(jnp.concatenate([f[-1:] for f in fields]), axis, up)
    above = lax.ppermute(jnp.concatenate([f[:1] for f in fields]), axis, down)
    return below, above


def conv_valid(planes, kernel):
    out = lax.conv_general_dilated(
        planes[None],
        kernel,
        (1, 1, 1),
        "VALID",
        dimension_numbers=("NDHWC", "DHWIO", "NDHWC"),
        preferred_element_type=jnp.float32,
    )
    return out[0]


def pad_sides(field):
    return jnp.pad(field, ((0, 0), (1, 1), (1, 1), (0, 0)))


def column_stack(padded):
    width = padded.shape[2] - 2
    return jnp.concatenate([padded[:, :, c:c + width, :] for c in range(3)], -1)


def weight_rows(local, halos, grads):
    height = grads.shape[1]
    xl = column_stack(local)
    xh = column_stack(halos)
    out = []
    for b in range(3):
        m = jnp.einsum("phwk,qhwo->pqko", xl[:, b:b + height], grads,
                       preferred_element_type=jnp.float32)
        mh = jnp.einsum("phwk,phwo->pko", xh[:, b:b + height], grads,
                        preferred_element_type=jnp.float32)
        out.append(jnp.stack((m[0, 1] + mh[0], m[0, 0] + m[1, 1], m[1, 0] + mh[1])))
    return jnp.stack(out, 1)


def stage_groups(bits):
    rest = list(range(1, bits))
    groups = [[0]]
    if len(rest) % 2:
        groups.append([rest.pop(0)])
    groups += [rest[j:j + 2] for j in range(0, len(rest), 2)]
    return groups


def halving_sum(x, axis, hold):
    count = lax.axis_size(axis)
    me = lax.axis_index(axis)
    bits = count.bit_length() - 1
    assert 1 << bits == count
    groups = stage_groups(bits)
    shape = x.shape
    flat = x.reshape(-1, shape[-1])
    rows = flat.shape[0]
    unit = count * 8
    padded_rows = -(-rows // unit) * unit
    flat = jnp.pad(flat, ((0, padded_rows - rows), (0, 0)))

    def mask(group, t):
        return sum(((t >> j) & 1) << b for j, b in enumerate(group))

    def slot(group):
        return sum(((me >> b) & 1) << j for j, b in enumerate(group))

    for group in groups:
        size = 1 << len(group)
        part = flat.shape[0] // size
        mine = slot(group)
        total = lax.dynamic_slice_in_dim(flat, mine * part, part, 0)
        for t in range(1, size):
            send = lax.dynamic_slice_in_dim(flat, (mine ^ t) * part, part, 0)
            pairs = [(i, i ^ mask(group, t)) for i in range(count)]
            total = total + lax.ppermute(send, axis, pairs)
        flat = total
    for group in reversed(groups):
        if group is groups[0]:
            flat, hold = lax.optimization_barrier((flat, hold))
        size = 1 << len(group)
        mine = slot(group)
        got = [flat] + [lax.ppermute(flat, axis, [(i, i ^ mask(group, t)) for i in range(count)])
                        for t in range(1, size)]
        if size == 2:
            flat = jnp.where(mine == 0, jnp.concatenate(got, 0),
                             jnp.concatenate(got[::-1], 0))
            continue
        blocks = []
        for j in range(size):
            block = got[0]
            for t in range(1, size):
                block = jnp.where((mine ^ t) == j, got[t], block)
            blocks.append(block)
        flat = jnp.concatenate(blocks, 0)
    return flat[:rows].reshape(shape), hold


def body(volume, kernel, grad_out):
    assert volume.shape[0] == 2
    below, above = neighbour_planes((volume, grad_out), "slab")
    vol_p = pad_sides(volume)
    grad_p = pad_sides(grad_out)
    vol_below, vol_above = pad_sides(below[0:1]), pad_sides(above[0:1])
    cells = lax.axis_size("slab") * grad_out.shape[0] * grad_out.shape[1] * grad_out.shape[2]
    factor = 1.0 / jnp.sqrt(jnp.float32(cells))
    rows = weight_rows(vol_p, jnp.concatenate((vol_below, vol_above)), grad_out)
    terms = rows.reshape(3, 3, 3, kernel.shape[3], kernel.shape[4]) * factor
    grad_below, grad_above = pad_sides(below[1:2]), pad_sides(above[1:2])
    activation = conv_valid(jnp.concatenate((vol_below, vol_p, vol_above)), kernel)
    flipped = jnp.swapaxes(kernel[::-1, ::-1, ::-1], 3, 4)
    input_grad = conv_valid(jnp.concatenate((grad_below, grad_p, grad_above)), flipped)
    activation = activation.astype(jnp.bfloat16)
    input_grad = input_grad.astype(jnp.bfloat16)
    weight_grad, (activation, input_grad) = halving_sum(terms, "slab", (activation, input_grad))
    return (activation, input_grad, weight_grad)


def solution(mesh):
    return jax.shard_map(
        body,
        mesh=mesh,
        in_specs=(
            P(("groups", "slab"), None, None, None),
            P(),
            P(("groups", "slab"), None, None, None),
        ),
        out_specs=(
            P(("groups", "slab"), None, None, None),
            P(("groups", "slab"), None, None, None),
            P("groups", None, None, None, None),
        ),
        check_vma=False,
    )
```

```python
import jax
import jax.numpy as jnp
from jax import lax
from jax.sharding import PartitionSpec as P


def neighbour_planes(fields, axis):
    count = lax.axis_size(axis)
    up = [(i, i + 1) for i in range(count - 1)]
    down = [(j, i) for i, j in up]
    below = lax.ppermute(jnp.concatenate([f[-1:] for f in fields]), axis, up)
    above = lax.ppermute(jnp.concatenate([f[:1] for f in fields]), axis, down)
    return below, above


def conv_valid(planes, kernel):
    out = lax.conv_general_dilated(
        planes[None],
        kernel,
        (1, 1, 1),
        "VALID",
        dimension_numbers=("NDHWC", "DHWIO", "NDHWC"),
        preferred_element_type=jnp.float32,
    )
    return out[0]


def pad_sides(field):
    return jnp.pad(field, ((0, 0), (1, 1), (1, 1), (0, 0)))


def column_stack(padded):
    width = padded.shape[2] - 2
    return jnp.concatenate([padded[:, :, c:c + width, :] for c in range(3)], -1)


def weight_rows(local, halos, grads):
    height = grads.shape[1]
    xl = column_stack(local)
    xh = column_stack(halos)
    out = []
    for b in range(3):
        m = jnp.einsum("phwk,qhwo->pqko", xl[:, b:b + height], grads,
                       preferred_element_type=jnp.float32)
        mh = jnp.einsum("phwk,phwo->pko", xh[:, b:b + height], grads,
                        preferred_element_type=jnp.float32)
        out.append(jnp.stack((m[0, 1] + mh[0], m[0, 0] + m[1, 1], m[1, 0] + mh[1])))
    return jnp.stack(out, 1)


def stage_groups(bits):
    rest = list(range(1, bits))
    groups = [[0]]
    if len(rest) % 2:
        groups.append([rest.pop(0)])
    groups += [rest[j:j + 2] for j in range(0, len(rest), 2)]
    return groups


def halving_sum(x, axis, hold, late, late_fn):
    count = lax.axis_size(axis)
    me = lax.axis_index(axis)
    bits = count.bit_length() - 1
    assert 1 << bits == count
    groups = stage_groups(bits)
    shape = x.shape
    flat = x.reshape(-1, shape[-1])
    rows = flat.shape[0]
    unit = count * 8
    padded_rows = -(-rows // unit) * unit
    flat = jnp.pad(flat, ((0, padded_rows - rows), (0, 0)))

    def mask(group, t):
        return sum(((t >> j) & 1) << b for j, b in enumerate(group))

    def slot(group):
        return sum(((me >> b) & 1) << j for j, b in enumerate(group))

    for group in groups:
        size = 1 << len(group)
        part = flat.shape[0] // size
        mine = slot(group)
        total = lax.dynamic_slice_in_dim(flat, mine * part, part, 0)
        for t in range(1, size):
            send = lax.dynamic_slice_in_dim(flat, (mine ^ t) * part, part, 0)
            pairs = [(i, i ^ mask(group, t)) for i in range(count)]
            total = total + lax.ppermute(send, axis, pairs)
        flat = total
    for group in reversed(groups):
        if group is groups[1]:
            flat, late = lax.optimization_barrier((flat, late))
            hold = hold + (late_fn(late),)
        if group is groups[0]:
            flat, hold = lax.optimization_barrier((flat, hold))
        size = 1 << len(group)
        mine = slot(group)
        got = [flat] + [lax.ppermute(flat, axis, [(i, i ^ mask(group, t)) for i in range(count)])
                        for t in range(1, size)]
        blocks = []
        for j in range(size):
            block = got[0]
            for t in range(1, size):
                block = jnp.where((mine ^ t) == j, got[t], block)
            blocks.append(block)
        flat = jnp.concatenate(blocks, 0)
    return flat[:rows].reshape(shape), hold


def body(volume, kernel, grad_out):
    assert volume.shape[0] == 2
    below, above = neighbour_planes((volume, grad_out), "slab")
    vol_p = pad_sides(volume)
    grad_p = pad_sides(grad_out)
    vol_below, vol_above = pad_sides(below[0:1]), pad_sides(above[0:1])
    cells = lax.axis_size("slab") * grad_out.shape[0] * grad_out.shape[1] * grad_out.shape[2]
    factor = 1.0 / jnp.sqrt(jnp.float32(cells))
    rows = weight_rows(vol_p, jnp.concatenate((vol_below, vol_above)), grad_out)
    terms = rows.reshape(3, 3, 3, kernel.shape[3], kernel.shape[4]) * factor
    grad_below, grad_above = pad_sides(below[1:2]), pad_sides(above[1:2])
    activation = conv_valid(jnp.concatenate((vol_below, vol_p, vol_above)), kernel)
    activation = activation.astype(jnp.bfloat16)
    flipped = jnp.swapaxes(kernel[::-1, ::-1, ::-1], 3, 4)
    grad_ext = jnp.concatenate((grad_below, grad_p, grad_above))

    def late_conv(field):
        return conv_valid(field, flipped).astype(jnp.bfloat16)

    weight_grad, (activation, input_grad) = halving_sum(
        terms, "slab", (activation,), grad_ext, late_conv)
    return (activation, input_grad, weight_grad)


def solution(mesh):
    return jax.shard_map(
        body,
        mesh=mesh,
        in_specs=(
            P(("groups", "slab"), None, None, None),
            P(),
            P(("groups", "slab"), None, None, None),
        ),
        out_specs=(
            P(("groups", "slab"), None, None, None),
            P(("groups", "slab"), None, None, None),
            P("groups", None, None, None, None),
        ),
        check_vma=False,
    )
```

```python
import jax
import jax.numpy as jnp
from jax import lax
from jax.sharding import PartitionSpec as P


def neighbour_planes(fields, axis):
    count = lax.axis_size(axis)
    up = [(i, i + 1) for i in range(count - 1)]
    down = [(j, i) for i, j in up]
    last = jnp.concatenate([f[-1:] for f in fields])
    first = jnp.concatenate([f[:1] for f in fields])
    below = lax.ppermute(last, axis, up)
    above = lax.ppermute(first, axis, down)
    fields, _ = lax.optimization_barrier((fields, (last, first)))
    return below, above, fields


def conv_valid(planes, kernel):
    out = lax.conv_general_dilated(
        planes[None],
        kernel,
        (1, 1, 1),
        "VALID",
        dimension_numbers=("NDHWC", "DHWIO", "NDHWC"),
        preferred_element_type=jnp.float32,
    )
    return out[0]


def pad_sides(field):
    return jnp.pad(field, ((0, 0), (1, 1), (1, 1), (0, 0)))


def column_stack(padded):
    width = padded.shape[2] - 2
    return jnp.concatenate([padded[:, :, c:c + width, :] for c in range(3)], -1)


def weight_rows(local, halos, grads):
    height = grads.shape[1]
    xl = column_stack(local)
    xh = column_stack(halos)
    out = []
    for b in range(3):
        m = jnp.einsum("phwk,qhwo->pqko", xl[:, b:b + height], grads,
                       preferred_element_type=jnp.float32)
        mh = jnp.einsum("phwk,phwo->pko", xh[:, b:b + height], grads,
                        preferred_element_type=jnp.float32)
        out.append(jnp.stack((m[0, 1] + mh[0], m[0, 0] + m[1, 1], m[1, 0] + mh[1])))
    return jnp.stack(out, 1)


def stage_groups(bits):
    rest = list(range(1, bits))
    groups = [[0]]
    if len(rest) % 2:
        groups.append([rest.pop(0)])
    groups += [rest[j:j + 2] for j in range(0, len(rest), 2)]
    return groups


def halving_sum(x, axis, hold):
    count = lax.axis_size(axis)
    me = lax.axis_index(axis)
    bits = count.bit_length() - 1
    assert 1 << bits == count
    groups = stage_groups(bits)
    shape = x.shape
    flat = x.reshape(-1, shape[-1])
    rows = flat.shape[0]
    unit = count * 8
    padded_rows = -(-rows // unit) * unit
    flat = jnp.pad(flat, ((0, padded_rows - rows), (0, 0)))

    def mask(group, t):
        return sum(((t >> j) & 1) << b for j, b in enumerate(group))

    def slot(group):
        return sum(((me >> b) & 1) << j for j, b in enumerate(group))

    for group in groups:
        size = 1 << len(group)
        part = flat.shape[0] // size
        mine = slot(group)
        total = lax.dynamic_slice_in_dim(flat, mine * part, part, 0)
        for t in range(1, size):
            send = lax.dynamic_slice_in_dim(flat, (mine ^ t) * part, part, 0)
            pairs = [(i, i ^ mask(group, t)) for i in range(count)]
            total = total + lax.ppermute(send, axis, pairs)
        flat = total
    for group in reversed(groups):
        if group is groups[0]:
            flat, hold = lax.optimization_barrier((flat, hold))
        size = 1 << len(group)
        mine = slot(group)
        got = [flat] + [lax.ppermute(flat, axis, [(i, i ^ mask(group, t)) for i in range(count)])
                        for t in range(1, size)]
        blocks = []
        for j in range(size):
            block = got[0]
            for t in range(1, size):
                block = jnp.where((mine ^ t) == j, got[t], block)
            blocks.append(block)
        flat = jnp.concatenate(blocks, 0)
    return flat[:rows].reshape(shape), hold


def body(volume, kernel, grad_out):
    assert volume.shape[0] == 2
    below, above, (volume, grad_out) = neighbour_planes((volume, grad_out), "slab")
    vol_p = pad_sides(volume)
    grad_p = pad_sides(grad_out)
    vol_below, vol_above = pad_sides(below[0:1]), pad_sides(above[0:1])
    cells = lax.axis_size("slab") * grad_out.shape[0] * grad_out.shape[1] * grad_out.shape[2]
    factor = 1.0 / jnp.sqrt(jnp.float32(cells))
    rows = weight_rows(vol_p, jnp.concatenate((vol_below, vol_above)), grad_out)
    terms = rows.reshape(3, 3, 3, kernel.shape[3], kernel.shape[4]) * factor
    grad_below, grad_above = pad_sides(below[1:2]), pad_sides(above[1:2])
    activation = conv_valid(jnp.concatenate((vol_below, vol_p, vol_above)), kernel)
    flipped = jnp.swapaxes(kernel[::-1, ::-1, ::-1], 3, 4)
    input_grad = conv_valid(jnp.concatenate((grad_below, grad_p, grad_above)), flipped)
    activation = activation.astype(jnp.bfloat16)
    input_grad = input_grad.astype(jnp.bfloat16)
    weight_grad, (activation, input_grad) = halving_sum(terms, "slab", (activation, input_grad))
    return (activation, input_grad, weight_grad)


def solution(mesh):
    return jax.shard_map(
        body,
        mesh=mesh,
        in_specs=(
            P(("groups", "slab"), None, None, None),
            P(),
            P(("groups", "slab"), None, None, None),
        ),
        out_specs=(
            P(("groups", "slab"), None, None, None),
            P(("groups", "slab"), None, None, None),
            P("groups", None, None, None, None),
        ),
        check_vma=False,
    )
```
